256 devices in a mesh: wide: 32 (over z, y), narrow: 8 (over x, core).
Axes of the slice: x: 4, y: 4, z: 8, core: 2. Of those that a mesh axis runs over, the one named last changes fastest.
Arguments:
- hidden: bfloat16 [65536, 8192], P('wide', 'narrow'), may hold values from -6 to 6
- base_key_value: bfloat16 [8192, 8, 2, 128], P('narrow'), may hold values from -0.0625 to 0.0625
- store_a: bfloat16 [256, 8192, 128], P('wide', 'narrow'), may hold values from -0.0625 to 0.0625
- stored_up_maps: bfloat16 [256, 2, 64, 8, 128], P('wide', None, None, 'narrow'), may hold values from -0.75 to 0.75
- adapter_ids: int32 [512], P('wide'), may hold values from 0 to 255, as said below
- span_start: int32 [512], P('wide'), may hold values from 0 to 31
Outputs:
- key_value: bfloat16 [8, 65536, 2, 128], P('narrow', 'wide')
The draws below stay inside these ranges and needn't reach their ends.
Inputs may be any that keep to these rules, and one draw needn't show every extreme that they name: `adapter_ids`: requests of one replica that name different adapters name adapters of different owners, the owner of adapter a being the replica a // 8.
All inputs are finite; a program needn't handle non-finite values.
Results may differ from the reference program's by a relative error of at most 0.015.
Values may be sent and summed in bfloat16 or wider, within the bound.
No kernel may reach another device: no remote copies, remote signals or barrier semaphores. Data moves between devices by JAX's collectives and lax.ppermute only.
A program may use at most 192 MiB of HBM per device.

```python
import jax
import jax.numpy as jnp
from jax import lax

MODEL_WIDTH = 8192
KEY_VALUE_HEADS = 8
HEAD_SIZE = 128
ADAPTER_RANK = 64
REQUEST_TOKENS = 128
REPLICA_REQUESTS = 16
ADAPT_DEV = 8
STORED_ADAPTERS = 256
NREQ = 512
TOKENS = 65536
N_WIDE = 32
N_NARROW = 8


def force_front(order, target, place):
    current = order[place]
    moved = jnp.where(order == target, current, order)
    return moved.at[place].set(target)


def draw_adapter_ids(key, part):
    subkeys = jax.random.split(jax.random.fold_in(key, 17), 3)
    row_keys = jax.random.split(subkeys[0], N_WIDE)
    owner_orders = jax.vmap(lambda subkey: jax.random.permutation(subkey, N_WIDE))(row_keys).astype(jnp.int32)
    first_row = force_front(owner_orders[0], jnp.int32(N_WIDE // 2), 0)
    first_row = force_front(first_row, jnp.int32(1), 1)
    second_row = force_front(owner_orders[1], jnp.int32(0), 0)
    owner_orders = owner_orders.at[0].set(first_row).at[1].set(second_row)
    slot_table = jnp.minimum(jax.random.randint(subkeys[1], (N_WIDE, N_WIDE), 0, ADAPT_DEV), jax.random.randint(subkeys[2], (N_WIDE, N_WIDE), 0, ADAPT_DEV))
    positions = jnp.arange(REPLICA_REQUESTS, dtype=jnp.int32) % N_WIDE
    owners = owner_orders[:, positions]
    slot_ids = slot_table[:, positions]
    picked = owners * ADAPT_DEV + slot_ids
    return picked.reshape(N_WIDE * REPLICA_REQUESTS).astype(jnp.int32)


def touch_ends(entries, rng, smallest, high):
    extent = entries.shape
    spot = [jax.random.randint(jax.random.fold_in(rng, axis), (), 0, extent[axis]) for axis in range(len(extent))]
    entries = entries.at[tuple(spot)].set(smallest)
    longest = extent.index(max(extent))
    spot[longest] = (spot[longest] + 1) % extent[longest]
    return entries.at[tuple(spot)].set(high)


def steps_of(own_key, extent, cuts, least, high):
    gain, own = 1.0, jax.random.fold_in(own_key, 6)
    for dim, blocks in cuts:
        steps = jnp.exp(jax.random.uniform(jax.random.fold_in(own, dim), (blocks,), jnp.float32, least / len(cuts), high / len(cuts)))
        gain = gain * jnp.repeat(steps, extent[dim] // blocks).reshape([-1 if axis == dim else 1 for axis in range(len(extent))])
    return gain


def centred(rng, dims, deviation, most, pieces=(), held_as=jnp.bfloat16):
    entries = deviation * jax.random.normal(rng, dims, jnp.float32)
    if pieces:
        entries = entries * steps_of(rng, dims, pieces, -0.22, 0.18)
    return jnp.clip(entries, -most, most).astype(held_as)


def setup_inputs(seed: int = 0) -> dict:
    streams_of = jax.random.split(jax.random.key(seed), 7)
    hidden = centred(streams_of[0], (TOKENS, MODEL_WIDTH), 1.0, 6.0, ((0, 32), (1, 8)))
    base_key_value = centred(streams_of[1], (MODEL_WIDTH, KEY_VALUE_HEADS, 2, HEAD_SIZE), MODEL_WIDTH ** -0.5, 0.0625, ((0, 8),))
    store_a = centred(streams_of[2], (STORED_ADAPTERS, MODEL_WIDTH, 2 * ADAPTER_RANK), MODEL_WIDTH ** -0.5, 0.0625, ((0, 32), (1, 8)))
    stored_up_maps = centred(streams_of[3], (STORED_ADAPTERS, 2, ADAPTER_RANK, KEY_VALUE_HEADS, HEAD_SIZE), ADAPTER_RANK ** -0.5, 0.75, ((0, 32), (3, 8)))
    adapter_ids = draw_adapter_ids(jax.random.fold_in(streams_of[6], 71), 0)
    span_start = touch_ends(jax.random.randint(streams_of[5], (NREQ,), 0, 32), jax.random.fold_in(streams_of[5], 1), 0, 31).astype(jnp.int32)
    return dict(hidden=hidden, base_key_value=base_key_value, store_a=store_a, stored_up_maps=stored_up_maps, adapter_ids=adapter_ids, span_start=span_start)


THETA = 500000.0


def rotate_keys(values, positions):
    half_dim = values.shape[-1] // 2
    frequency = THETA ** (-(jnp.arange(half_dim, dtype=jnp.float32) * 2.0 / values.shape[-1]))
    angles = positions[:, None] * frequency[None, :]
    angles = jnp.concatenate([angles, angles], axis=-1)
    turned = jnp.concatenate([-values[..., half_dim:], values[..., :half_dim]], axis=-1)
    return values * jnp.cos(angles) + turned * jnp.sin(angles)


def reference(hidden, base_key_value, store_a, stored_up_maps, adapter_ids, span_start):
    local_width = MODEL_WIDTH // N_NARROW
    weight_float_copy = base_key_value.astype(jnp.float32).reshape(N_NARROW, local_width, KEY_VALUE_HEADS * 2 * HEAD_SIZE)

    def per_request(request):
        request = request.astype(jnp.int32)
        rows = lax.dynamic_slice_in_dim(hidden, request * REQUEST_TOKENS, REQUEST_TOKENS, 0)
        split_rows = rows.astype(jnp.float32).reshape(REQUEST_TOKENS, N_NARROW, local_width)
        partial_sums = jnp.einsum('tnd,ndc->ntc', split_rows, weight_float_copy)
        partial_sums = lax.optimization_barrier(partial_sums.astype(jnp.bfloat16)).astype(jnp.float32)
        base_total_sum = jnp.sum(partial_sums, axis=0).reshape(REQUEST_TOKENS, KEY_VALUE_HEADS, 2, HEAD_SIZE)
        adapter_a = store_a[adapter_ids[request]]
        adapter_b = stored_up_maps[adapter_ids[request]]
        shrunk = jnp.dot(rows, adapter_a, preferred_element_type=jnp.float32).astype(jnp.bfloat16)
        shrunk = shrunk.reshape(REQUEST_TOKENS, 2, ADAPTER_RANK)
        delta = jnp.einsum('tjk,jkhc->thjc', shrunk.astype(jnp.float32), adapter_b.astype(jnp.float32))
        raw = base_total_sum + delta
        positions = (span_start[request] * REQUEST_TOKENS + jnp.arange(REQUEST_TOKENS, dtype=jnp.int32)).astype(jnp.float32)
        keys_turned = jax.vmap(lambda head_keys: rotate_keys(head_keys, positions), in_axes=1, out_axes=1)(raw[:, :, 0, :])
        joined = jnp.stack([keys_turned, raw[:, :, 1, :]], axis=2)
        return joined.astype(jnp.bfloat16)

    token_blocks = lax.map(per_request, jnp.arange(N_WIDE * REPLICA_REQUESTS, dtype=jnp.int32))
    token_blocks = token_blocks.reshape(N_WIDE * REPLICA_REQUESTS * REQUEST_TOKENS, KEY_VALUE_HEADS, 2, HEAD_SIZE)
    return jnp.transpose(token_blocks, (1, 0, 2, 3))
```

```python
import jax
import jax.numpy as jnp
from jax import lax
from jax.sharding import PartitionSpec as P


THETA = 500000.0


def rotate_keys(values, positions):
    half_dim = values.shape[-1] // 2
    frequency = THETA ** (-(jnp.arange(half_dim, dtype=jnp.float32) * 2.0 / values.shape[-1]))
    angles = positions[:, None] * frequency[None, :]
    angles = jnp.concatenate([angles, angles], axis=-1)
    turned = jnp.concatenate([-values[..., half_dim:], values[..., :half_dim]], axis=-1)
    return values * jnp.cos(angles) + turned * jnp.sin(angles)


def shards(hidden, base_key_value, store_a, stored_up_maps, adapter_ids, span_start):
    wide_count = lax.axis_size("wide")
    me = lax.axis_index("wide")
    stored = store_a.shape[0]
    requests = adapter_ids.shape[0]
    span_len = hidden.shape[0] // requests
    width = store_a.shape[1]
    rank_two = store_a.shape[2]
    rank = rank_two // 2
    heads_here = stored_up_maps.shape[3]
    head_size = stored_up_maps.shape[4]

    all_ids = lax.all_gather(adapter_ids, "wide", tiled=True).reshape(wide_count, requests)
    asked = all_ids // stored == me
    chosen = jnp.max(jnp.where(asked, all_ids % stored, 0), axis=1)

    up_rows = stored_up_maps.reshape(stored, 2 * rank * heads_here, head_size)
    packed = jnp.concatenate([store_a, up_rows], axis=1)
    reply = packed[chosen]
    got = lax.all_to_all(reply, "wide", split_axis=0, concat_axis=0, tiled=True)

    partials = jnp.einsum(
        "td,dhjc->htjc", hidden, base_key_value, preferred_element_type=jnp.float32
    ).astype(jnp.bfloat16)
    base_total_sum = lax.psum_scatter(
        partials, "narrow", scatter_dimension=0, tiled=True
    )
    got, base_total_sum = lax.optimization_barrier((got, base_total_sum))
    base_total_sum = base_total_sum.astype(jnp.float32)

    owners = adapter_ids // stored
    needed = got[owners]
    needed_a = needed[:, :width]
    needed_b = needed[:, width:].reshape(requests, 2, rank, heads_here, head_size)
    request_rows = hidden.reshape(requests, span_len, hidden.shape[1])
    shrink_part = jnp.einsum(
        "rtd,rdc->rtc", request_rows, needed_a, preferred_element_type=jnp.float32
    )
    shrunk = lax.psum(shrink_part.astype(jnp.bfloat16), "narrow")
    shrunk_split = shrunk.reshape(requests, span_len, 2, rank)
    delta = jnp.einsum(
        "rtjk,rjkhc->hrtjc", shrunk_split, needed_b, preferred_element_type=jnp.float32
    )
    raw = base_total_sum + delta.reshape(base_total_sum.shape)
    positions = (
        (span_start[:, None] * span_len + jnp.arange(span_len, dtype=jnp.int32)[None, :])
        .reshape(-1)
        .astype(jnp.float32)
    )
    keys_turned = jax.vmap(lambda head_keys: rotate_keys(head_keys, positions))(raw[:, :, 0, :])
    joined = jnp.stack([keys_turned, raw[:, :, 1, :]], axis=2)
    return joined.astype(jnp.bfloat16)


def solution(mesh):
    placed = (
        P("wide", "narrow"),
        P("narrow", None, None, None),
        P("wide", "narrow", None),
        P("wide", None, None, "narrow", None),
        P("wide"),
        P("wide"),
    )
    return jax.shard_map(
        shards,
        mesh=mesh,
        in_specs=placed,
        out_specs=P("narrow", "wide", None, None),
        check_vma=False,
    )
```

```python
import jax
import jax.numpy as jnp
from jax import lax
from jax.sharding import PartitionSpec as P


THETA = 500000.0


def rotate_keys(values, positions):
    half_dim = values.shape[-1] // 2
    frequency = THETA ** (-(jnp.arange(half_dim, dtype=jnp.float32) * 2.0 / values.shape[-1]))
    angles = positions[:, None] * frequency[None, :]
    angles = jnp.concatenate([angles, angles], axis=-1)
    turned = jnp.concatenate([-values[..., half_dim:], values[..., :half_dim]], axis=-1)
    return values * jnp.cos(angles) + turned * jnp.sin(angles)


def shards(hidden, base_key_value, store_a, stored_up_maps, adapter_ids, span_start):
    wide_count = lax.axis_size("wide")
    stored = store_a.shape[0]
    requests = adapter_ids.shape[0]
    span_len = hidden.shape[0] // requests
    width = store_a.shape[1]
    rank_two = store_a.shape[2]
    rank = rank_two // 2
    heads_here = stored_up_maps.shape[3]
    head_size = stored_up_maps.shape[4]

    owners = adapter_ids // stored
    matches = owners[None, :] == jnp.arange(wide_count, dtype=jnp.int32)[:, None]
    wanted = jnp.max(jnp.where(matches, adapter_ids % stored, 0), axis=1)
    chosen = lax.all_to_all(
        wanted.reshape(wide_count, 1), "wide", split_axis=0, concat_axis=0, tiled=True
    )[:, 0]

    up_rows = stored_up_maps.reshape(stored, 2 * rank * heads_here, head_size)
    packed = jnp.concatenate([store_a, up_rows], axis=1)
    reply = packed[chosen]
    got = lax.all_to_all(reply, "wide", split_axis=0, concat_axis=0, tiled=True)

    partials = jnp.einsum(
        "td,dhjc->htjc", hidden, base_key_value, preferred_element_type=jnp.float32
    ).astype(jnp.bfloat16)
    base_total_sum = lax.psum_scatter(
        partials, "narrow", scatter_dimension=0, tiled=True
    )
    got, base_total_sum = lax.optimization_barrier((got, base_total_sum))
    base_total_sum = base_total_sum.astype(jnp.float32)

    needed = got[owners]
    needed_a = needed[:, :width]
    needed_b = needed[:, width:].reshape(requests, 2, rank, heads_here, head_size)
    request_rows = hidden.reshape(requests, span_len, hidden.shape[1])
    shrink_part = jnp.einsum(
        "rtd,rdc->rtc", request_rows, needed_a, preferred_element_type=jnp.float32
    )
    shrunk = lax.psum(shrink_part, "narrow").astype(jnp.bfloat16)
    shrunk_split = shrunk.reshape(requests, span_len, 2, rank)
    delta = jnp.einsum(
        "rtjk,rjkhc->hrtjc", shrunk_split, needed_b, preferred_element_type=jnp.float32
    )
    raw = base_total_sum + delta.reshape(base_total_sum.shape)
    positions = (
        (span_start[:, None] * span_len + jnp.arange(span_len, dtype=jnp.int32)[None, :])
        .reshape(-1)
        .astype(jnp.float32)
    )
    keys_turned = jax.vmap(lambda head_keys: rotate_keys(head_keys, positions))(raw[:, :, 0, :])
    joined = jnp.stack([keys_turned, raw[:, :, 1, :]], axis=2)
    return joined.astype(jnp.bfloat16)


def solution(mesh):
    placed = (
        P("wide", "narrow"),
        P("narrow", None, None, None),
        P("wide", "narrow", None),
        P("wide", None, None, "narrow", None),
        P("wide"),
        P("wide"),
    )
    return jax.shard_map(
        shards,
        mesh=mesh,
        in_specs=placed,
        out_specs=P("narrow", "wide", None, None),
        check_vma=False,
    )
```

```python
import jax
import jax.numpy as jnp
from jax import lax
from jax.sharding import PartitionSpec as P


THETA = 500000.0


def rotate_keys(values, positions):
    half_dim = values.shape[-1] // 2
    frequency = THETA ** (-(jnp.arange(half_dim, dtype=jnp.float32) * 2.0 / values.shape[-1]))
    angles = positions[:, None] * frequency[None, :]
    angles = jnp.concatenate([angles, angles], axis=-1)
    turned = jnp.concatenate([-values[..., half_dim:], values[..., :half_dim]], axis=-1)
    return values * jnp.cos(angles) + turned * jnp.sin(angles)


def narrow_sum(v):
    count = lax.axis_size("narrow")
    me = lax.axis_index("narrow")
    bits = []
    bit = 1
    while bit < count:
        bits.append(bit)
        bit *= 2
    cur = v
    for bit in bits:
        half = cur.shape[0] // 2
        upper = (me & bit) > 0
        send = jnp.where(upper, cur[:half], cur[half:])
        keep = jnp.where(upper, cur[half:], cur[:half])
        pairs = [(i, i ^ bit) for i in range(count)]
        cur = keep + lax.ppermute(send, "narrow", pairs)
    cur = cur.astype(jnp.bfloat16)
    for bit in reversed(bits):
        upper = (me & bit) > 0
        pairs = [(i, i ^ bit) for i in range(count)]
        other = lax.ppermute(cur, "narrow", pairs)
        cur = jnp.where(
            upper, jnp.concatenate([other, cur]), jnp.concatenate([cur, other])
        )
    return cur


def shards(hidden, base_key_value, store_a, stored_up_maps, adapter_ids, span_start):
    wide_count = lax.axis_size("wide")
    stored = store_a.shape[0]
    requests = adapter_ids.shape[0]
    span_len = hidden.shape[0] // requests
    width = store_a.shape[1]
    rank_two = store_a.shape[2]
    rank = rank_two // 2
    heads_here = stored_up_maps.shape[3]
    head_size = stored_up_maps.shape[4]

    owners = adapter_ids // stored
    matches = owners[None, :] == jnp.arange(wide_count, dtype=jnp.int32)[:, None]
    wanted = jnp.max(jnp.where(matches, adapter_ids % stored, 0), axis=1)
    chosen = lax.all_to_all(
        wanted.reshape(wide_count, 1), "wide", split_axis=0, concat_axis=0, tiled=True
    )[:, 0]

    up_rows = stored_up_maps.reshape(stored, 2 * rank * heads_here, head_size)
    packed = jnp.concatenate([store_a, up_rows], axis=1)
    reply = packed[chosen]
    got = lax.all_to_all(reply, "wide", split_axis=0, concat_axis=0, tiled=True)

    partials = jnp.einsum(
        "td,dhjc->htjc", hidden, base_key_value, preferred_element_type=jnp.float32
    ).astype(jnp.bfloat16)
    base_total_sum = lax.psum_scatter(
        partials, "narrow", scatter_dimension=0, tiled=True
    )
    got, base_total_sum = lax.optimization_barrier((got, base_total_sum))
    base_total_sum = base_total_sum.astype(jnp.float32)

    needed = got[owners]
    needed_a = needed[:, :width]
    needed_b = needed[:, width:].reshape(requests, 2, rank, heads_here, head_size)
    request_rows = hidden.reshape(requests, span_len, hidden.shape[1])
    shrink_part = jnp.einsum(
        "rtd,rdc->rtc", request_rows, needed_a, preferred_element_type=jnp.float32
    )
    shrunk = narrow_sum(shrink_part.reshape(requests * span_len, rank_two))
    shrunk_split = shrunk.reshape(requests, span_len, 2, rank)
    delta = jnp.einsum(
        "rtjk,rjkhc->hrtjc", shrunk_split, needed_b, preferred_element_type=jnp.float32
    )
    raw = base_total_sum + delta.reshape(base_total_sum.shape)
    positions = (
        (span_start[:, None] * span_len + jnp.arange(span_len, dtype=jnp.int32)[None, :])
        .reshape(-1)
        .astype(jnp.float32)
    )
    keys_turned = jax.vmap(lambda head_keys: rotate_keys(head_keys, positions))(raw[:, :, 0, :])
    joined = jnp.stack([keys_turned, raw[:, :, 1, :]], axis=2)
    return joined.astype(jnp.bfloat16)


def solution(mesh):
    placed = (
        P("wide", "narrow"),
        P("narrow", None, None, None),
        P("wide", "narrow", None),
        P("wide", None, None, "narrow", None),
        P("wide"),
        P("wide"),
    )
    return jax.shard_map(
        shards,
        mesh=mesh,
        in_specs=placed,
        out_specs=P("narrow", "wide", None, None),
        check_vma=False,
    )
```

```python
import jax
import jax.numpy as jnp
from jax import lax
from jax.experimental import pallas as pl
from jax.experimental.pallas import tpu as pltpu
from jax.sharding import PartitionSpec as P


THETA = 500000.0


def narrow_sum(v):
    count = lax.axis_size("narrow")
    me = lax.axis_index("narrow")
    bits = []
    bit = 1
    while bit < count:
        bits.append(bit)
        bit *= 2
    cur = v
    for bit in bits:
        half = cur.shape[0] // 2
        upper = (me & bit) > 0
        send = jnp.where(upper, cur[:half], cur[half:])
        keep = jnp.where(upper, cur[half:], cur[:half])
        pairs = [(i, i ^ bit) for i in range(count)]
        cur = keep + lax.ppermute(send, "narrow", pairs)
    cur = cur.astype(jnp.bfloat16)
    for bit in reversed(bits):
        upper = (me & bit) > 0
        pairs = [(i, i ^ bit) for i in range(count)]
        other = lax.ppermute(cur, "narrow", pairs)
        cur = jnp.where(
            upper, jnp.concatenate([other, cur]), jnp.concatenate([cur, other])
        )
    return cur


def shrink_body(owner_ref, rows_ref, maps_ref, out_ref):
    width = rows_ref.shape[1]
    out_ref[...] = jnp.dot(
        rows_ref[...], maps_ref[0, :width, :], preferred_element_type=jnp.float32
    )


def shrink(owners, hidden, got):
    requests = owners.shape[0]
    span_len = hidden.shape[0] // requests
    rows = got.shape[1]
    rank_two = got.shape[2]
    return pl.pallas_call(
        shrink_body,
        grid_spec=pltpu.PrefetchScalarGridSpec(
            num_scalar_prefetch=1,
            grid=(requests,),
            in_specs=[
                pl.BlockSpec((span_len, hidden.shape[1]), lambda r, own: (r, 0)),
                pl.BlockSpec((1, rows, rank_two), lambda r, own: (own[r], 0, 0)),
            ],
            out_specs=pl.BlockSpec((span_len, rank_two), lambda r, own: (r, 0)),
        ),
        out_shape=jax.ShapeDtypeStruct((hidden.shape[0], rank_two), jnp.float32),
    )(owners, hidden, got)


def finish_body(owner_ref, base_ref, shrunk_ref, up_ref, cos_ref, sin_ref, out_ref):
    rank_two = up_ref.shape[1]
    head_size = up_ref.shape[2]
    up = up_ref[0]
    row = lax.broadcasted_iota(jnp.int32, up.shape, 0)
    zero = jnp.zeros_like(up)
    keys_up = jnp.where(row < rank_two // 2, up, zero)
    values_up = jnp.where(row < rank_two // 2, zero, up)
    both_up = jnp.concatenate([keys_up, values_up], axis=1)
    delta = jnp.dot(shrunk_ref[...], both_up, preferred_element_type=jnp.float32)
    raw = base_ref[...].astype(jnp.float32) + delta
    keys = raw[:, :head_size]
    turned = pltpu.roll(keys, head_size // 2, 1)
    keys = keys * cos_ref[...] + turned * sin_ref[...]
    out_ref[...] = jnp.concatenate([keys, raw[:, head_size:]], axis=1).astype(out_ref.dtype)


def finish(owners, base, shrunk, got, cos, sin):
    requests = owners.shape[0]
    tokens = base.shape[0]
    span_len = tokens // requests
    rank_two = got.shape[2]
    up_block = got.shape[1] // rank_two - 1
    head_size = cos.shape[1]
    return pl.pallas_call(
        finish_body,
        grid_spec=pltpu.PrefetchScalarGridSpec(
            num_scalar_prefetch=1,
            grid=(requests,),
            in_specs=[
                pl.BlockSpec((span_len, base.shape[1]), lambda r, own: (r, 0)),
                pl.BlockSpec((span_len, rank_two), lambda r, own: (r, 0)),
                pl.BlockSpec(
                    (1, rank_two, rank_two), lambda r, own: (own[r], up_block, 0)
                ),
                pl.BlockSpec((span_len, head_size), lambda r, own: (r, 0)),
                pl.BlockSpec((span_len, head_size), lambda r, own: (r, 0)),
            ],
            out_specs=pl.BlockSpec((span_len, base.shape[1]), lambda r, own: (r, 0)),
        ),
        out_shape=jax.ShapeDtypeStruct(base.shape, jnp.bfloat16),
    )(owners, base, shrunk, got, cos, sin)


def rotation_tables(span_start, span_len, head_size):
    half_dim = head_size // 2
    positions = (
        (span_start[:, None] * span_len + jnp.arange(span_len, dtype=jnp.int32)[None, :])
        .reshape(-1)
        .astype(jnp.float32)
    )
    frequency = THETA ** (-(jnp.arange(half_dim, dtype=jnp.float32) * 2.0 / head_size))
    angles = positions[:, None] * frequency[None, :]
    cos = jnp.cos(angles)
    sin = jnp.sin(angles)
    return jnp.concatenate([cos, cos], axis=-1), jnp.concatenate([-sin, sin], axis=-1)


def shards(hidden, base_key_value, store_a, stored_up_maps, adapter_ids, span_start):
    wide_count = lax.axis_size("wide")
    stored = store_a.shape[0]
    requests = adapter_ids.shape[0]
    span_len = hidden.shape[0] // requests
    rank_two = store_a.shape[2]
    heads_here = stored_up_maps.shape[3]
    head_size = stored_up_maps.shape[4]

    owners = adapter_ids // stored
    matches = owners[None, :] == jnp.arange(wide_count, dtype=jnp.int32)[:, None]
    wanted = jnp.max(jnp.where(matches, adapter_ids % stored, 0), axis=1)
    chosen = lax.all_to_all(
        wanted.reshape(wide_count, 1), "wide", split_axis=0, concat_axis=0, tiled=True
    )[:, 0]

    up_rows = stored_up_maps.reshape(stored, rank_two * heads_here, head_size)
    packed = jnp.concatenate([store_a, up_rows], axis=1)
    reply = packed[chosen]
    got = lax.all_to_all(reply, "wide", split_axis=0, concat_axis=0, tiled=True)

    partials = jnp.einsum(
        "td,dhjc->htjc", hidden, base_key_value, preferred_element_type=jnp.float32
    ).astype(jnp.bfloat16)
    base_total_sum = lax.psum_scatter(
        partials, "narrow", scatter_dimension=0, tiled=True
    )
    got, base_total_sum = lax.optimization_barrier((got, base_total_sum))

    shrink_part = shrink(owners, hidden, got)
    shrunk = narrow_sum(shrink_part)
    cos, sin = rotation_tables(span_start, span_len, head_size)
    base_rows = base_total_sum.reshape(hidden.shape[0], 2 * head_size)
    joined = finish(owners, base_rows, shrunk, got, cos, sin)
    return joined.reshape(base_total_sum.shape)


def solution(mesh):
    placed = (
        P("wide", "narrow"),
        P("narrow", None, None, None),
        P("wide", "narrow", None),
        P("wide", None, None, "narrow", None),
        P("wide"),
        P("wide"),
    )
    return jax.shard_map(
        shards,
        mesh=mesh,
        in_specs=placed,
        out_specs=P("narrow", "wide", None, None),
        check_vma=False,
    )
```

```python
import jax
import jax.numpy as jnp
from jax import lax
from jax.sharding import PartitionSpec as P


THETA = 500000.0


def rotate_keys(values, positions):
    half_dim = values.shape[-1] // 2
    frequency = THETA ** (-(jnp.arange(half_dim, dtype=jnp.float32) * 2.0 / values.shape[-1]))
    angles = positions[:, None] * frequency[None, :]
    angles = jnp.concatenate([angles, angles], axis=-1)
    turned = jnp.concatenate([-values[..., half_dim:], values[..., :half_dim]], axis=-1)
    return values * jnp.cos(angles) + turned * jnp.sin(angles)


def narrow_sum(v):
    count = lax.axis_size("narrow")
    me = lax.axis_index("narrow")
    bits = []
    bit = 1
    while bit < count:
        bits.append(bit)
        bit *= 2
    cur = v
    for bit in bits:
        half = cur.shape[0] // 2
        upper = (me & bit) > 0
        send = jnp.where(upper, cur[:half], cur[half:])
        keep = jnp.where(upper, cur[half:], cur[:half])
        pairs = [(i, i ^ bit) for i in range(count)]
        cur = keep + lax.ppermute(send, "narrow", pairs)
    cur = cur.astype(jnp.bfloat16)
    for bit in reversed(bits):
        upper = (me & bit) > 0
        pairs = [(i, i ^ bit) for i in range(count)]
        other = lax.ppermute(cur, "narrow", pairs)
        cur = jnp.where(
            upper, jnp.concatenate([other, cur]), jnp.concatenate([cur, other])
        )
    return cur


def shards(hidden, base_key_value, store_a, stored_up_maps, adapter_ids, span_start):
    wide_count = lax.axis_size("wide")
    stored = store_a.shape[0]
    requests = adapter_ids.shape[0]
    span_len = hidden.shape[0] // requests
    width = store_a.shape[1]
    rank_two = store_a.shape[2]
    rank = rank_two // 2
    heads_here = stored_up_maps.shape[3]
    head_size = stored_up_maps.shape[4]

    owners = adapter_ids // stored
    matches = owners[None, :] == jnp.arange(wide_count, dtype=jnp.int32)[:, None]
    wanted = jnp.max(jnp.where(matches, adapter_ids % stored, 0), axis=1)
    chosen = lax.all_to_all(
        wanted.reshape(wide_count, 1), "wide", split_axis=0, concat_axis=0, tiled=True
    )[:, 0]

    up_rows = stored_up_maps.reshape(stored, 2 * rank * heads_here, head_size)
    packed = jnp.concatenate([store_a, up_rows], axis=1)
    reply = packed[chosen]
    got = lax.all_to_all(reply, "wide", split_axis=0, concat_axis=0, tiled=True)

    tokens = hidden.shape[0]
    heads = base_key_value.shape[1]
    flat_w = base_key_value.reshape(width, heads * 2 * head_size)
    partials = jnp.dot(hidden, flat_w, preferred_element_type=jnp.float32)
    partials = partials.astype(jnp.bfloat16).reshape(tokens, heads, 2 * head_size)
    partials = partials.transpose(1, 0, 2)
    base_total_sum = lax.psum_scatter(
        partials, "narrow", scatter_dimension=0, tiled=True
    )
    got, base_total_sum = lax.optimization_barrier((got, base_total_sum))

    needed = got[owners]
    needed_a = needed[:, :width]
    up = needed[:, width:]
    request_rows = hidden.reshape(requests, span_len, hidden.shape[1])
    shrink_part = jnp.einsum(
        "rtd,rdc->rtc", request_rows, needed_a, preferred_element_type=jnp.float32
    )
    shrunk = narrow_sum(shrink_part.reshape(requests * span_len, rank_two))
    row = lax.broadcasted_iota(jnp.int32, up.shape, 1)
    zero = jnp.zeros_like(up)
    both_up = jnp.concatenate(
        [jnp.where(row < rank, up, zero), jnp.where(row < rank, zero, up)], axis=2
    )
    delta = jnp.einsum(
        "rtk,rkc->rtc",
        shrunk.reshape(requests, span_len, rank_two),
        both_up,
        preferred_element_type=jnp.float32,
    ).reshape(tokens, 2 * head_size)
    raw = base_total_sum.reshape(tokens, 2 * head_size).astype(jnp.float32) + delta
    positions = (
        (span_start[:, None] * span_len + jnp.arange(span_len, dtype=jnp.int32)[None, :])
        .reshape(-1)
        .astype(jnp.float32)
    )
    keys_turned = rotate_keys(raw[:, :head_size], positions)
    joined = jnp.concatenate([keys_turned, raw[:, head_size:]], axis=1)
    return joined.astype(jnp.bfloat16).reshape(base_total_sum.shape[0], tokens, 2, head_size)


def solution(mesh):
    placed = (
        P("wide", "narrow"),
        P("narrow", None, None, None),
        P("wide", "narrow", None),
        P("wide", None, None, "narrow", None),
        P("wide"),
        P("wide"),
    )
    return jax.shard_map(
        shards,
        mesh=mesh,
        in_specs=placed,
        out_specs=P("narrow", "wide", None, None),
        check_vma=False,
    )
```

```python
import jax
import jax.numpy as jnp
from jax import lax
from jax.sharding import PartitionSpec as P


THETA = 500000.0


def rotate_keys(values, positions):
    half_dim = values.shape[-1] // 2
    frequency = THETA ** (-(jnp.arange(half_dim, dtype=jnp.float32) * 2.0 / values.shape[-1]))
    angles = positions[:, None] * frequency[None, :]
    angles = jnp.concatenate([angles, angles], axis=-1)
    turned = jnp.concatenate([-values[..., half_dim:], values[..., :half_dim]], axis=-1)
    return values * jnp.cos(angles) + turned * jnp.sin(angles)


def narrow_sum(v):
    count = lax.axis_size("narrow")
    me = lax.axis_index("narrow")
    bits = []
    bit = 1
    while bit < count:
        bits.append(bit)
        bit *= 2
    cur = v
    for bit in bits:
        half = cur.shape[0] // 2
        upper = (me & bit) > 0
        send = jnp.where(upper, cur[:half], cur[half:])
        keep = jnp.where(upper, cur[half:], cur[:half])
        pairs = [(i, i ^ bit) for i in range(count)]
        cur = keep + lax.ppermute(send, "narrow", pairs)
    cur = cur.astype(jnp.bfloat16)
    for bit in reversed(bits):
        upper = (me & bit) > 0
        pairs = [(i, i ^ bit) for i in range(count)]
        other = lax.ppermute(cur, "narrow", pairs)
        cur = jnp.where(
            upper, jnp.concatenate([other, cur]), jnp.concatenate([cur, other])
        )
    return cur


def narrow_scatter(v):
    count = lax.axis_size("narrow")
    me = lax.axis_index("narrow")
    cur = v
    bit = 1
    while bit < count:
        pairs = [(i, i ^ bit) for i in range(count)]
        halves = cur.reshape(cur.shape[0] // 2, 2, *cur.shape[1:])
        keep = (me // bit) % 2
        mine = lax.dynamic_index_in_dim(halves, keep, axis=1, keepdims=False)
        theirs = lax.dynamic_index_in_dim(halves, 1 - keep, axis=1, keepdims=False)
        cur = mine.astype(jnp.float32) + lax.ppermute(theirs, "narrow", pairs).astype(
            jnp.float32
        )
        bit *= 2
    return cur


def shards(hidden, base_key_value, store_a, stored_up_maps, adapter_ids, span_start):
    wide_count = lax.axis_size("wide")
    stored = store_a.shape[0]
    requests = adapter_ids.shape[0]
    span_len = hidden.shape[0] // requests
    width = store_a.shape[1]
    rank_two = store_a.shape[2]
    rank = rank_two // 2
    heads_here = stored_up_maps.shape[3]
    head_size = stored_up_maps.shape[4]

    owners = adapter_ids // stored
    matches = owners[None, :] == jnp.arange(wide_count, dtype=jnp.int32)[:, None]
    wanted = jnp.max(jnp.where(matches, adapter_ids % stored, 0), axis=1)
    chosen = lax.all_to_all(
        wanted.reshape(wide_count, 1), "wide", split_axis=0, concat_axis=0, tiled=True
    )[:, 0]

    up_rows = stored_up_maps.reshape(stored, 2 * rank * heads_here, head_size)
    packed = jnp.concatenate([store_a, up_rows], axis=1)
    reply = packed[chosen]
    got = lax.all_to_all(reply, "wide", split_axis=0, concat_axis=0, tiled=True)

    tokens = hidden.shape[0]
    heads = base_key_value.shape[1]
    flat_w = base_key_value.reshape(width, heads * 2 * head_size)
    partials = jnp.dot(hidden, flat_w, preferred_element_type=jnp.float32)
    partials = partials.astype(jnp.bfloat16).reshape(tokens, heads, 2 * head_size)
    partials = partials.transpose(1, 0, 2)
    base_total_sum = narrow_scatter(partials)
    got, base_total_sum = lax.optimization_barrier((got, base_total_sum))

    needed = got[owners]
    needed_a = needed[:, :width]
    up = needed[:, width:]
    request_rows = hidden.reshape(requests, span_len, hidden.shape[1])
    shrink_part = jnp.einsum(
        "rtd,rdc->rtc", request_rows, needed_a, preferred_element_type=jnp.float32
    )
    shrunk = narrow_sum(shrink_part.reshape(requests * span_len, rank_two))
    row = lax.broadcasted_iota(jnp.int32, up.shape, 1)
    zero = jnp.zeros_like(up)
    both_up = jnp.concatenate(
        [jnp.where(row < rank, up, zero), jnp.where(row < rank, zero, up)], axis=2
    )
    delta = jnp.einsum(
        "rtk,rkc->rtc",
        shrunk.reshape(requests, span_len, rank_two),
        both_up,
        preferred_element_type=jnp.float32,
    ).reshape(tokens, 2 * head_size)
    raw = base_total_sum.reshape(tokens, 2 * head_size).astype(jnp.float32) + delta
    positions = (
        (span_start[:, None] * span_len + jnp.arange(span_len, dtype=jnp.int32)[None, :])
        .reshape(-1)
        .astype(jnp.float32)
    )
    keys_turned = rotate_keys(raw[:, :head_size], positions)
    joined = jnp.concatenate([keys_turned, raw[:, head_size:]], axis=1)
    return joined.astype(jnp.bfloat16).reshape(base_total_sum.shape[0], tokens, 2, head_size)


def solution(mesh):
    placed = (
        P("wide", "narrow"),
        P("narrow", None, None, None),
        P("wide", "narrow", None),
        P("wide", None, None, "narrow", None),
        P("wide"),
        P("wide"),
    )
    return jax.shard_map(
        shards,
        mesh=mesh,
        in_specs=placed,
        out_specs=P("narrow", "wide", None, None),
        check_vma=False,
    )
```

```python
import jax
import jax.numpy as jnp
from jax import lax
from jax.sharding import PartitionSpec as P


THETA = 500000.0


def rotate_keys(values, positions):
    half_dim = values.shape[-1] // 2
    frequency = THETA ** (-(jnp.arange(half_dim, dtype=jnp.float32) * 2.0 / values.shape[-1]))
    angles = positions[:, None] * frequency[None, :]
    angles = jnp.concatenate([angles, angles], axis=-1)
    turned = jnp.concatenate([-values[..., half_dim:], values[..., :half_dim]], axis=-1)
    return values * jnp.cos(angles) + turned * jnp.sin(angles)


def narrow_sum(v):
    count = lax.axis_size("narrow")
    me = lax.axis_index("narrow")
    bits = []
    bit = 1
    while bit < count:
        bits.append(bit)
        bit *= 2
    cur = v
    for bit in bits[:-1]:
        half = cur.shape[0] // 2
        upper = (me & bit) > 0
        send = jnp.where(upper, cur[:half], cur[half:])
        keep = jnp.where(upper, cur[half:], cur[:half])
        pairs = [(i, i ^ bit) for i in range(count)]
        cur = keep + lax.ppermute(send, "narrow", pairs)
    if bits:
        pairs = [(i, i ^ bits[-1]) for i in range(count)]
        cur = cur + lax.ppermute(cur, "narrow", pairs)
    cur = cur.astype(jnp.bfloat16)
    for bit in reversed(bits[:-1]):
        upper = (me & bit) > 0
        pairs = [(i, i ^ bit) for i in range(count)]
        other = lax.ppermute(cur, "narrow", pairs)
        cur = jnp.where(
            upper, jnp.concatenate([other, cur]), jnp.concatenate([cur, other])
        )
    return cur


def narrow_scatter(v):
    count = lax.axis_size("narrow")
    me = lax.axis_index("narrow")
    cur = v
    bit = 1
    while bit < count:
        pairs = [(i, i ^ bit) for i in range(count)]
        halves = cur.reshape(cur.shape[0] // 2, 2, *cur.shape[1:])
        keep = (me // bit) % 2
        mine = lax.dynamic_index_in_dim(halves, keep, axis=1, keepdims=False)
        theirs = lax.dynamic_index_in_dim(halves, 1 - keep, axis=1, keepdims=False)
        cur = mine.astype(jnp.float32) + lax.ppermute(theirs, "narrow", pairs).astype(
            jnp.float32
        )
        bit *= 2
    return cur


def shards(hidden, base_key_value, store_a, stored_up_maps, adapter_ids, span_start):
    wide_count = lax.axis_size("wide")
    stored = store_a.shape[0]
    requests = adapter_ids.shape[0]
    span_len = hidden.shape[0] // requests
    width = store_a.shape[1]
    rank_two = store_a.shape[2]
    rank = rank_two // 2
    heads_here = stored_up_maps.shape[3]
    head_size = stored_up_maps.shape[4]

    owners = adapter_ids // stored
    matches = owners[None, :] == jnp.arange(wide_count, dtype=jnp.int32)[:, None]
    wanted = jnp.max(jnp.where(matches, adapter_ids % stored, 0), axis=1)
    chosen = lax.all_to_all(
        wanted.reshape(wide_count, 1), "wide", split_axis=0, concat_axis=0, tiled=True
    )[:, 0]

    up_rows = stored_up_maps.reshape(stored, 2 * rank * heads_here, head_size)
    packed = jnp.concatenate([store_a, up_rows], axis=1)
    reply = packed[chosen]
    got = lax.all_to_all(reply, "wide", split_axis=0, concat_axis=0, tiled=True)

    tokens = hidden.shape[0]
    heads = base_key_value.shape[1]
    flat_w = base_key_value.reshape(width, heads * 2 * head_size)
    partials = jnp.dot(hidden, flat_w, preferred_element_type=jnp.float32)
    partials = partials.astype(jnp.bfloat16).reshape(tokens, heads, 2 * head_size)
    partials = partials.transpose(1, 0, 2)
    base_total_sum = narrow_scatter(partials)
    got, base_total_sum = lax.optimization_barrier((got, base_total_sum))

    needed = jnp.stack(
        [lax.dynamic_index_in_dim(got, owners[r], keepdims=False) for r in range(requests)]
    )
    needed_a = needed[:, :width]
    up = needed[:, width:]
    request_rows = hidden.reshape(requests, span_len, hidden.shape[1])
    shrink_part = jnp.einsum(
        "rtd,rdc->rtc", request_rows, needed_a, preferred_element_type=jnp.float32
    )
    shrunk = narrow_sum(shrink_part.reshape(requests * span_len, rank_two))
    row = lax.broadcasted_iota(jnp.int32, up.shape, 1)
    zero = jnp.zeros_like(up)
    both_up = jnp.concatenate(
        [jnp.where(row < rank, up, zero), jnp.where(row < rank, zero, up)], axis=2
    )
    delta = jnp.einsum(
        "rtk,rkc->rtc",
        shrunk.reshape(requests, span_len, rank_two),
        both_up,
        preferred_element_type=jnp.float32,
    ).reshape(tokens, 2 * head_size)
    raw = base_total_sum.reshape(tokens, 2 * head_size).astype(jnp.float32) + delta
    positions = (
        (span_start[:, None] * span_len + jnp.arange(span_len, dtype=jnp.int32)[None, :])
        .reshape(-1)
        .astype(jnp.float32)
    )
    keys_turned = rotate_keys(raw[:, :head_size], positions)
    joined = jnp.concatenate([keys_turned, raw[:, head_size:]], axis=1)
    return joined.astype(jnp.bfloat16).reshape(base_total_sum.shape[0], tokens, 2, head_size)


def solution(mesh):
    placed = (
        P("wide", "narrow"),
        P("narrow", None, None, None),
        P("wide", "narrow", None),
        P("wide", None, None, "narrow", None),
        P("wide"),
        P("wide"),
    )
    return jax.shard_map(
        shards,
        mesh=mesh,
        in_specs=placed,
        out_specs=P("narrow", "wide", None, None),
        check_vma=False,
    )
```

```python
import jax
import jax.numpy as jnp
from jax import lax
from jax.sharding import PartitionSpec as P


THETA = 500000.0


def narrow_sum(v):
    count = lax.axis_size("narrow")
    me = lax.axis_index("narrow")
    bits = []
    bit = 1
    while bit < count:
        bits.append(bit)
        bit *= 2
    cur = v
    for bit in bits[:-1]:
        half = cur.shape[0] // 2
        upper = (me & bit) > 0
        send = jnp.where(upper, cur[:half], cur[half:])
        keep = jnp.where(upper, cur[half:], cur[:half])
        pairs = [(i, i ^ bit) for i in range(count)]
        cur = keep + lax.ppermute(send, "narrow", pairs)
    if bits:
        pairs = [(i, i ^ bits[-1]) for i in range(count)]
        cur = cur + lax.ppermute(cur, "narrow", pairs)
    cur = cur.astype(jnp.bfloat16)
    for bit in reversed(bits[:-1]):
        upper = (me & bit) > 0
        pairs = [(i, i ^ bit) for i in range(count)]
        other = lax.ppermute(cur, "narrow", pairs)
        cur = jnp.where(
            upper, jnp.concatenate([other, cur]), jnp.concatenate([cur, other])
        )
    return cur


def narrow_scatter(v):
    count = lax.axis_size("narrow")
    me = lax.axis_index("narrow")
    cur = v
    bit = 1
    while bit < count:
        pairs = [(i, i ^ bit) for i in range(count)]
        halves = cur.reshape(cur.shape[0] // 2, 2, *cur.shape[1:])
        keep = (me // bit) % 2
        mine = lax.dynamic_index_in_dim(halves, keep, axis=1, keepdims=False)
        theirs = lax.dynamic_index_in_dim(halves, 1 - keep, axis=1, keepdims=False)
        cur = mine.astype(jnp.float32) + lax.ppermute(theirs, "narrow", pairs).astype(
            jnp.float32
        )
        bit *= 2
    return cur


def shards(hidden, base_key_value, store_a, stored_up_maps, adapter_ids, span_start):
    wide_count = lax.axis_size("wide")
    stored = store_a.shape[0]
    requests = adapter_ids.shape[0]
    span_len = hidden.shape[0] // requests
    width = store_a.shape[1]
    rank_two = store_a.shape[2]
    rank = rank_two // 2
    heads_here = stored_up_maps.shape[3]
    head_size = stored_up_maps.shape[4]

    owners = adapter_ids // stored
    matches = owners[None, :] == jnp.arange(wide_count, dtype=jnp.int32)[:, None]
    wanted = jnp.max(jnp.where(matches, adapter_ids % stored, 0), axis=1)
    chosen = lax.all_to_all(
        wanted.reshape(wide_count, 1), "wide", split_axis=0, concat_axis=0, tiled=True
    )[:, 0]

    up_rows = stored_up_maps.reshape(stored, 2 * rank * heads_here, head_size)
    packed = jnp.concatenate([store_a, up_rows], axis=1)
    reply = packed[chosen]
    got = lax.all_to_all(reply, "wide", split_axis=0, concat_axis=0, tiled=True)

    tokens = hidden.shape[0]
    heads = base_key_value.shape[1]
    flat_w = base_key_value.reshape(width, heads * 2 * head_size)
    partials = jnp.dot(hidden, flat_w, preferred_element_type=jnp.float32)
    partials = partials.astype(jnp.bfloat16).reshape(tokens, heads, 2 * head_size)
    partials = partials.transpose(1, 0, 2)
    base_total_sum = narrow_scatter(partials)
    positions = (
        (span_start[:, None] * span_len + jnp.arange(span_len, dtype=jnp.int32)[None, :])
        .reshape(-1)
        .astype(jnp.float32)
    )
    half_dim = head_size // 2
    frequency = THETA ** (-(jnp.arange(half_dim, dtype=jnp.float32) * 2.0 / head_size))
    angles = positions[:, None] * frequency[None, :]
    angles = jnp.concatenate([angles, angles], axis=-1)
    got, base_total_sum, cos, sin = lax.optimization_barrier(
        (got, base_total_sum, jnp.cos(angles), jnp.sin(angles))
    )

    needed = got[owners]
    needed_a = needed[:, :width]
    up = needed[:, width:]
    request_rows = hidden.reshape(requests, span_len, hidden.shape[1])
    shrink_part = jnp.einsum(
        "rtd,rdc->rtc", request_rows, needed_a, preferred_element_type=jnp.float32
    )
    shrunk = narrow_sum(shrink_part.reshape(requests * span_len, rank_two))
    row = lax.broadcasted_iota(jnp.int32, up.shape, 1)
    zero = jnp.zeros_like(up)
    both_up = jnp.concatenate(
        [jnp.where(row < rank, up, zero), jnp.where(row < rank, zero, up)], axis=2
    )
    delta = jnp.einsum(
        "rtk,rkc->rtc",
        shrunk.reshape(requests, span_len, rank_two),
        both_up,
        preferred_element_type=jnp.float32,
    ).reshape(tokens, 2 * head_size)
    raw = base_total_sum.reshape(tokens, 2 * head_size).astype(jnp.float32) + delta
    keys = raw[:, :head_size]
    turned = jnp.concatenate([-keys[:, half_dim:], keys[:, :half_dim]], axis=-1)
    keys_turned = keys * cos + turned * sin
    joined = jnp.concatenate([keys_turned, raw[:, head_size:]], axis=1)
    return joined.astype(jnp.bfloat16).reshape(base_total_sum.shape[0], tokens, 2, head_size)


def solution(mesh):
    placed = (
        P("wide", "narrow"),
        P("narrow", None, None, None),
        P("wide", "narrow", None),
        P("wide", None, None, "narrow", None),
        P("wide"),
        P("wide"),
    )
    return jax.shard_map(
        shards,
        mesh=mesh,
        in_specs=placed,
        out_specs=P("narrow", "wide", None, None),
        check_vma=False,
    )
```

```python
import jax
import jax.numpy as jnp
from jax import lax
from jax.sharding import PartitionSpec as P


THETA = 500000.0


def narrow_sum(v):
    count = lax.axis_size("narrow")
    me = lax.axis_index("narrow")
    bits = []
    bit = 1
    while bit < count:
        bits.append(bit)
        bit *= 2
    cur = v
    for bit in bits[:-1]:
        half = cur.shape[0] // 2
        upper = (me // bit) % 2
        send = lax.dynamic_slice_in_dim(cur, (1 - upper) * half, half)
        keep = lax.dynamic_slice_in_dim(cur, upper * half, half)
        pairs = [(i, i ^ bit) for i in range(count)]
        cur = keep + lax.ppermute(send, "narrow", pairs)
    if bits:
        pairs = [(i, i ^ bits[-1]) for i in range(count)]
        cur = cur + lax.ppermute(cur, "narrow", pairs)
    cur = cur.astype(jnp.bfloat16)
    for bit in reversed(bits[:-1]):
        upper = (me & bit) > 0
        pairs = [(i, i ^ bit) for i in range(count)]
        other = lax.ppermute(cur, "narrow", pairs)
        cur = jnp.where(
            upper, jnp.concatenate([other, cur]), jnp.concatenate([cur, other])
        )
    return cur


def narrow_scatter(v):
    count = lax.axis_size("narrow")
    me = lax.axis_index("narrow")
    cur = v
    bit = 1
    while bit < count:
        pairs = [(i, i ^ bit) for i in range(count)]
        halves = cur.reshape(cur.shape[0] // 2, 2, *cur.shape[1:])
        keep = (me // bit) % 2
        mine = lax.dynamic_index_in_dim(halves, keep, axis=1, keepdims=False)
        theirs = lax.dynamic_index_in_dim(halves, 1 - keep, axis=1, keepdims=False)
        cur = mine.astype(jnp.float32) + lax.ppermute(theirs, "narrow", pairs).astype(
            jnp.float32
        )
        bit *= 2
    return cur


def shards(hidden, base_key_value, store_a, stored_up_maps, adapter_ids, span_start):
    wide_count = lax.axis_size("wide")
    stored = store_a.shape[0]
    requests = adapter_ids.shape[0]
    span_len = hidden.shape[0] // requests
    width = store_a.shape[1]
    rank_two = store_a.shape[2]
    rank = rank_two // 2
    heads_here = stored_up_maps.shape[3]
    head_size = stored_up_maps.shape[4]

    owners = adapter_ids // stored
    matches = owners[None, :] == jnp.arange(wide_count, dtype=jnp.int32)[:, None]
    wanted = jnp.max(jnp.where(matches, adapter_ids % stored, 0), axis=1)
    chosen = lax.all_to_all(
        wanted.reshape(wide_count, 1), "wide", split_axis=0, concat_axis=0, tiled=True
    )[:, 0]

    up_rows = stored_up_maps.reshape(stored, 2 * rank * heads_here, head_size)
    packed = jnp.concatenate([store_a, up_rows], axis=1)
    reply = packed[chosen]
    got = lax.all_to_all(reply, "wide", split_axis=0, concat_axis=0, tiled=True)

    tokens = hidden.shape[0]
    heads = base_key_value.shape[1]
    flat_w = base_key_value.reshape(width, heads * 2 * head_size)
    partials = jnp.dot(hidden, flat_w, preferred_element_type=jnp.float32)
    partials = partials.astype(jnp.bfloat16).reshape(tokens, heads, 2 * head_size)
    partials = partials.transpose(1, 0, 2)
    base_total_sum = narrow_scatter(partials)
    positions = (
        (span_start[:, None] * span_len + jnp.arange(span_len, dtype=jnp.int32)[None, :])
        .reshape(-1)
        .astype(jnp.float32)
    )
    half_dim = head_size // 2
    frequency = THETA ** (-(jnp.arange(half_dim, dtype=jnp.float32) * 2.0 / head_size))
    angles = positions[:, None] * frequency[None, :]
    angles = jnp.concatenate([angles, angles], axis=-1)
    got, base_total_sum, cos, sin = lax.optimization_barrier(
        (got, base_total_sum, jnp.cos(angles), jnp.sin(angles))
    )

    needed = got[owners]
    needed_a = needed[:, :width]
    up = needed[:, width:]
    request_rows = hidden.reshape(requests, span_len, hidden.shape[1])
    shrink_part = jnp.einsum(
        "rtd,rdc->rtc", request_rows, needed_a, preferred_element_type=jnp.float32
    )
    shrunk = narrow_sum(shrink_part.reshape(requests * span_len, rank_two))
    row = lax.broadcasted_iota(jnp.int32, up.shape, 1)
    zero = jnp.zeros_like(up)
    both_up = jnp.concatenate(
        [jnp.where(row < rank, up, zero), jnp.where(row < rank, zero, up)], axis=2
    )
    delta = jnp.einsum(
        "rtk,rkc->rtc",
        shrunk.reshape(requests, span_len, rank_two),
        both_up,
        preferred_element_type=jnp.float32,
    ).reshape(tokens, 2 * head_size)
    raw = base_total_sum.reshape(tokens, 2 * head_size).astype(jnp.float32) + delta
    keys = raw[:, :head_size]
    turned = jnp.concatenate([-keys[:, half_dim:], keys[:, :half_dim]], axis=-1)
    keys_turned = keys * cos + turned * sin
    joined = jnp.concatenate([keys_turned, raw[:, head_size:]], axis=1)
    return joined.astype(jnp.bfloat16).reshape(base_total_sum.shape[0], tokens, 2, head_size)


def solution(mesh):
    placed = (
        P("wide", "narrow"),
        P("narrow", None, None, None),
        P("wide", "narrow", None),
        P("wide", None, None, "narrow", None),
        P("wide"),
        P("wide"),
    )
    return jax.shard_map(
        shards,
        mesh=mesh,
        in_specs=placed,
        out_specs=P("narrow", "wide", None, None),
        check_vma=False,
    )
```
